256 devices in a mesh: view: 8 (over x, y_lo), tile: 32 (over z, y_hi, core).
Axes of the slice: x: 4, y: 4 (y_hi: 2, y_lo: 2; y = y_hi * 2 + y_lo), z: 8, core: 2. Of those that a mesh axis runs over, the one named last changes fastest.
Arguments:
- latents: bfloat16 [16, 2048, 1536], P('view', 'tile'), may hold values from -14 to 14
- qkv_weight: bfloat16 [1536, 3072], replicated, may hold values from -0.15625 to 0.15625
- out_weight: bfloat16 [1024, 1536], replicated, may hold values from -0.1875 to 0.1875
- anchor: int32 [1], replicated, may hold values from 0 to 15
- epi_list: int32 [16, 16, 6], P('view'), may hold values from -1 to 31, as said below
Outputs:
- attn_out: bfloat16 [16, 2048, 1536], P('view', 'tile')
The draws below stay inside these ranges and needn't reach their ends.
Inputs may be any that keep to these rules, and one draw needn't show every extreme that they name: `epi_list`: row (v, b) lists distinct key blocks: an id c < 16 is block c of view (v - 1) mod 16, an id c >= 16 is block c - 16 of view (v + 1) mod 16; unused slots hold -1 and follow the used ones. Every row uses 1 to 6 slots, with a cap that varies from view to view, and some row uses all 6.
All inputs are finite; a program needn't handle non-finite values.
Results may differ from the reference program's by a relative error of at most 0.005.
The reference program's roundings to bfloat16 on the way (of `projected`, `joined`, `weights` and `attended`) count: a program that leaves them out, or rounds other values in their place, can miss the bound.
Values may be sent and summed in bfloat16 or wider, within the bound.
No kernel may reach another device: no remote copies, remote signals or barrier semaphores. Data moves between devices by JAX's collectives and lax.ppermute only.
A program may use at most 128 MiB of HBM per device.

```python
import math
import jax
import jax.numpy as jnp
from jax import lax

D = 1536
HEADS = 8
HD = 128
VIEWS = 16
VT = 2048
BLK = 128
EMAX = 6
NBLK = 16


def draw_latents(key, part):
    key_one = jax.random.fold_in(key, 0)
    values = jax.random.normal(key_one, (VIEWS, VT, D), jnp.float32)
    return jnp.clip(values, -14.0, 14.0).astype(jnp.bfloat16)


def draw_epi_list(key, part):
    key_order, key_room, key_count, key_full = jax.random.split(key, 4)
    candidates = 2 * NBLK
    ranking = jax.random.randint(key_order, (VIEWS, NBLK, candidates), 0, 1 << 20) * candidates + jnp.arange(candidates, dtype=jnp.int32)
    chosen = jnp.argsort(ranking, axis=-1)[..., :EMAX].astype(jnp.int32)
    room = jax.random.randint(key_room, (VIEWS, 1), 1, EMAX + 1)
    counts = 1 + jax.random.randint(key_count, (VIEWS, NBLK), 0, room)
    fullest = jax.random.randint(key_full, (), 0, VIEWS)
    view_ids = jnp.arange(VIEWS, dtype=jnp.int32)[:, None]
    block_ids = jnp.arange(NBLK, dtype=jnp.int32)[None, :]
    counts = jnp.where((view_ids == fullest) & (block_ids == 0), EMAX, counts)
    slots = jnp.arange(EMAX, dtype=jnp.int32)
    return jnp.where(slots[None, None, :] < counts[..., None], chosen, -1).astype(jnp.int32)


def centred(stream_key, shape, deviation, limit, kind=jnp.bfloat16):
    result = deviation * jax.random.normal(stream_key, shape, jnp.float32)
    return jnp.clip(result, min=-limit, max=limit).astype(kind)


def setup_inputs(seed: int = 0) -> dict:
    streams_of = jax.random.split(jax.random.key(seed), 6)
    return {
        "latents": draw_latents(jax.random.fold_in(streams_of[5], 71), 0),
        "qkv_weight": centred(streams_of[1], (D, HEADS * 3 * HD), D ** -0.5, 0.15625),
        "out_weight": centred(streams_of[2], (HEADS * HD, D), (HEADS * HD) ** -0.5, 0.1875),
        "anchor": jax.random.randint(streams_of[3], (1,), 0, VIEWS).astype(jnp.int32),
        "epi_list": draw_epi_list(jax.random.fold_in(streams_of[5], 71), 0),
    }


def allowed_tokens(epi_rows):
    blocks = jnp.any(epi_rows[:, :, None] == jnp.arange(2 * NBLK, dtype=jnp.int32)[None, None, :], axis=1)
    nearby = jnp.repeat(jnp.repeat(blocks, BLK, axis=0), BLK, axis=1)
    always = jnp.ones((VT, VT), dtype=bool)
    return jnp.concatenate([always, nearby, always], axis=1)

def attend(queries, keys_part, values_part, allowed):
    scores = jnp.einsum('qd,kd->qk', queries.astype(jnp.float32), keys_part.astype(jnp.float32)) / math.sqrt(HD)
    scores = jnp.where(allowed, scores, -jnp.inf)
    row_peak = lax.optimization_barrier(jnp.max(scores, axis=1, keepdims=True))
    raised = jnp.exp(scores - row_peak)
    row_total = lax.optimization_barrier(jnp.sum(raised, axis=1, keepdims=True))
    weights = raised.astype(jnp.bfloat16)
    summed = jnp.einsum('qk,kd->qd', weights.astype(jnp.float32), values_part.astype(jnp.float32))
    return (summed / row_total).astype(jnp.bfloat16)

def reference(latents, qkv_weight, out_weight, anchor, epi_list):
    shaped = qkv_weight.reshape(D, HEADS, 3 * HD).astype(jnp.float32)

    def project(tokens):
        return jnp.einsum('td,dhc->htc', tokens.astype(jnp.float32), shaped).astype(jnp.bfloat16)
    projected = lax.map(project, latents)
    key_values = projected[..., HD:]
    anchored = lax.dynamic_index_in_dim(key_values, anchor[0].astype(jnp.int32), 0, keepdims=False)
    mixing = out_weight.reshape(HEADS, HD, D).astype(jnp.float32)

    def one_view(view_id):
        earlier = lax.dynamic_index_in_dim(key_values, ((view_id - 1) % VIEWS).astype(jnp.int32), 0, keepdims=False)
        following = lax.dynamic_index_in_dim(key_values, ((view_id + 1) % VIEWS).astype(jnp.int32), 0, keepdims=False)
        resident = lax.dynamic_index_in_dim(projected, view_id, 0, keepdims=False)
        joined = jnp.concatenate([resident[..., HD:], earlier, following, anchored], axis=1)
        allowed = allowed_tokens(lax.dynamic_index_in_dim(epi_list, view_id, 0, keepdims=False))

        def one_head(head_items):
            queries, keyvals = head_items
            return attend(queries, keyvals[:, :HD], keyvals[:, HD:], allowed)
        attended = lax.map(one_head, (resident[..., :HD], joined))
        return jnp.einsum('htc,hcd->td', attended.astype(jnp.float32), mixing).astype(jnp.bfloat16)
    return lax.map(one_view, jnp.arange(VIEWS, dtype=jnp.int32))
```

```python
import math

import jax
import jax.numpy as jnp
from jax import lax
from jax.sharding import Mesh
from jax.sharding import PartitionSpec as P

HEADS = 8
HD = 128
VT = 2048
BLK = 128
NBLK = 16

SUB = ("zh", "zl", "yhi", "core")
HALF = ("zl", "yhi", "core")


def allowed_tokens(epi_rows, rows):
    blocks = jnp.any(
        epi_rows[:, :, None] == jnp.arange(2 * NBLK, dtype=jnp.int32)[None, None, :], axis=1
    )
    nearby = jnp.repeat(jnp.repeat(blocks, BLK, axis=0), BLK, axis=1)
    always = jnp.ones((rows, VT), dtype=bool)
    return jnp.concatenate([always, nearby, always], axis=1)


def attend(queries, keys_part, values_part, allowed):
    scores = jnp.einsum(
        "qd,kd->qk", queries, keys_part, preferred_element_type=jnp.float32
    ) / math.sqrt(HD)
    scores = jnp.where(allowed, scores, -jnp.inf)
    row_peak = jnp.max(scores, axis=1, keepdims=True)
    raised = jnp.exp(scores - row_peak)
    row_total = jnp.sum(raised, axis=1, keepdims=True)
    weights = raised.astype(jnp.bfloat16)
    summed = jnp.einsum("qk,kd->qd", weights, values_part, preferred_element_type=jnp.float32)
    return (summed / row_total).astype(jnp.bfloat16)


def broadcast_view(value, root, count):
    me = lax.axis_index("view")
    dist = (me - root) % count
    held = jnp.where(dist == 0, value, jnp.zeros_like(value))
    step = 1
    while step < count:
        got = lax.ppermute(held, "view", [(i, (i + step) % count) for i in range(count)])
        held = jnp.where((dist >= step) & (dist < 2 * step), got, held)
        step *= 2
    return held


def body(latents, qkv_weight, out_weight, anchor, epi_list):
    per_dev, tile_tokens, model_width = latents.shape
    views_n = lax.axis_size("view")
    half_n = lax.axis_size(HALF)
    tile_n = lax.axis_size(SUB)
    part_rows = tile_tokens * half_n
    core_n = lax.axis_size("core")
    slot = lax.axis_index("core")
    half = lax.axis_index("zh")

    shaped = qkv_weight.reshape(model_width, HEADS, 3 * HD)
    projected = jnp.einsum(
        "vtd,dhc->hvtc", latents, shaped, preferred_element_type=jnp.float32
    ).astype(jnp.bfloat16)
    queries = projected[..., :HD]
    key_values = projected[..., HD:]

    target = anchor[0]
    anchor_tile = lax.dynamic_index_in_dim(key_values, target % per_dev, 1, keepdims=False)
    anchor_tile = broadcast_view(anchor_tile, target // per_dev, views_n)

    q_send = queries.reshape(HEADS * per_dev, tile_tokens, HD)
    q_mine = lax.all_to_all(q_send, HALF, 0, 0, tiled=True).reshape(part_rows, HD)

    kv_send = jnp.concatenate(
        [key_values, jnp.broadcast_to(anchor_tile[:, None], key_values.shape)], axis=-1
    ).reshape(HEADS * per_dev, tile_tokens, 4 * HD)
    kv_send = jnp.broadcast_to(kv_send[None], (tile_n // (HEADS * per_dev),) + kv_send.shape)
    kv_send = kv_send.reshape(tile_n, tile_tokens, 4 * HD)
    kv_all = lax.all_to_all(kv_send, SUB, 0, 0, tiled=True).reshape(tile_n * tile_tokens, 4 * HD)
    own_kv = kv_all[:, : 2 * HD]
    anchored = kv_all[:, 2 * HD :]

    other = lax.ppermute(own_kv, "core", [(0, 1), (1, 0)])
    pairs = []
    for v in range(views_n):
        for c in range(core_n):
            dest_view = (v + 1) % views_n if c == 1 else (v - 1) % views_n
            pairs.append((v * core_n + c, dest_view * core_n + (1 - c)))
    far = lax.ppermute(own_kv, ("view", "core"), pairs)
    earlier = jnp.where(slot == 1, other, far)
    following = jnp.where(slot == 1, far, other)

    epi_rows = lax.dynamic_index_in_dim(epi_list, slot, 0, keepdims=False)
    epi_rows = lax.dynamic_slice_in_dim(epi_rows, half * (part_rows // BLK), part_rows // BLK, 0)
    allowed = allowed_tokens(epi_rows, part_rows)
    joined = jnp.concatenate([own_kv, earlier, following, anchored], axis=0)

    block_rows = min(512, part_rows)
    block_count = part_rows // block_rows
    q_blocks = q_mine.reshape(block_count, block_rows, HD)
    mask_blocks = allowed.reshape(block_count, block_rows, 4 * VT)

    def one_block(items):
        query_rows, block_mask = items
        return attend(query_rows, joined[:, :HD], joined[:, HD:], block_mask)

    attended = lax.map(one_block, (q_blocks, mask_blocks)).reshape(half_n, tile_tokens, HD)
    returned = lax.all_to_all(attended, HALF, 0, 0, tiled=True)
    returned = returned.reshape(HEADS, per_dev, tile_tokens, HD)
    projected_out = jnp.einsum(
        "hvtc,hcd->vtd",
        returned,
        out_weight.reshape(HEADS, HD, model_width),
        preferred_element_type=jnp.float32,
    )
    return projected_out.astype(jnp.bfloat16)


def solution(mesh):
    views_n, tile_n = mesh.devices.shape
    fine = Mesh(
        mesh.devices.reshape(views_n, 2, tile_n // 8, 2, 2),
        ("view",) + SUB,
    )
    return jax.shard_map(
        body,
        mesh=fine,
        in_specs=(P("view", SUB, None), P(), P(), P(), P("view", None, None)),
        out_specs=P("view", SUB, None),
        check_vma=False,
    )
```

```python
import math

import jax
import jax.numpy as jnp
from jax import lax
from jax.experimental import pallas as pl
from jax.experimental.pallas import tpu as pltpu
from jax.sharding import Mesh
from jax.sharding import PartitionSpec as P

HEADS = 8
HD = 128
VT = 2048
BLK = 128
NBLK = 16

SUB = ("zh", "zl", "yhi", "core")
HALF = ("zl", "yhi", "core")


def attention_kernel(epi_ref, q_ref, own_ref, anc_ref, *rest):
    block = pl.program_id(0)
    nb_refs, o_ref = rest[:-1], rest[-1]
    queries = q_ref[...]
    scale = math.sqrt(HD)

    def scores_of(keyvals):
        return lax.dot_general(
            queries, keyvals[:, :HD], (((1,), (1,)), ((), ())),
            preferred_element_type=jnp.float32,
        ) / scale

    parts = []
    for ref in (own_ref, anc_ref):
        keyvals = ref[...]
        parts.append((scores_of(keyvals), keyvals))
    for slot, nb_ref in enumerate(nb_refs):
        index = epi_ref[block, slot]
        keyvals = nb_ref[...]
        scores = jnp.where(index >= 0, scores_of(keyvals), -jnp.inf)
        parts.append((scores, keyvals))
    peak = parts[0][0].max(axis=1, keepdims=True)
    for scores, _ in parts[1:]:
        peak = jnp.maximum(peak, scores.max(axis=1, keepdims=True))
    total = None
    summed = None
    for scores, keyvals in parts:
        raised = jnp.exp(scores - peak)
        row = raised.sum(axis=1, keepdims=True)
        prod = jnp.dot(raised.astype(jnp.bfloat16), keyvals[:, HD:], preferred_element_type=jnp.float32)
        total = row if total is None else total + row
        summed = prod if summed is None else summed + prod
    o_ref[...] = (summed / total).astype(o_ref.dtype)


def attention(epi_rows, queries, own, anchored, nearby):
    rows = queries.shape[0]
    spec_full = lambda n: pl.BlockSpec((n, 2 * HD), lambda b, epi: (0, 0))

    def spec_slot(slot):
        return pl.BlockSpec(
            (BLK, 2 * HD), lambda b, epi: (jnp.clip(epi[b, slot], 0, 2 * NBLK - 1), 0)
        )

    slots = epi_rows.shape[1]
    return pl.pallas_call(
        attention_kernel,
        out_shape=jax.ShapeDtypeStruct((rows, HD), jnp.bfloat16),
        grid_spec=pltpu.PrefetchScalarGridSpec(
            num_scalar_prefetch=1,
            grid=(rows // BLK,),
            in_specs=[
                pl.BlockSpec((BLK, HD), lambda b, epi: (b, 0)),
                spec_full(own.shape[0]),
                spec_full(anchored.shape[0]),
            ] + [spec_slot(e) for e in range(slots)],
            out_specs=pl.BlockSpec((BLK, HD), lambda b, epi: (b, 0)),
        ),
    )(epi_rows, queries, own, anchored, *([nearby] * slots))


def broadcast_view(value, root, count):
    me = lax.axis_index("view")
    dist = (me - root) % count
    held = jnp.where(dist == 0, value, jnp.zeros_like(value))
    step = 1
    while step < count:
        got = lax.ppermute(held, "view", [(i, (i + step) % count) for i in range(count)])
        held = jnp.where((dist >= step) & (dist < 2 * step), got, held)
        step *= 2
    return held


def body(latents, qkv_weight, out_weight, anchor, epi_list):
    per_dev, tile_tokens, model_width = latents.shape
    views_n = lax.axis_size("view")
    half_n = lax.axis_size(HALF)
    tile_n = lax.axis_size(SUB)
    part_rows = tile_tokens * half_n
    core_n = lax.axis_size("core")
    slot = lax.axis_index("core")
    half = lax.axis_index("zh")

    flat = jnp.dot(
        latents.reshape(per_dev * tile_tokens, model_width), qkv_weight,
        preferred_element_type=jnp.float32,
    ).astype(jnp.bfloat16)
    projected = flat.reshape(per_dev, tile_tokens, HEADS, 3 * HD).transpose(2, 0, 1, 3)
    queries = projected[..., :HD]
    key_values = projected[..., HD:]

    target = anchor[0]
    anchor_tile = lax.dynamic_index_in_dim(key_values, target % per_dev, 1, keepdims=False)
    anchor_tile = broadcast_view(anchor_tile, target // per_dev, views_n)

    q_send = queries.reshape(HEADS * per_dev, tile_tokens, HD)
    q_mine = lax.all_to_all(q_send, HALF, 0, 0, tiled=True).reshape(part_rows, HD)

    def to_units(source):
        wide = jnp.broadcast_to(source[None], (tile_n // (HEADS * per_dev),) + source.shape)
        wide = wide.reshape(tile_n, tile_tokens, 2 * HD)
        return lax.all_to_all(wide, SUB, 0, 0, tiled=True).reshape(tile_n * tile_tokens, 2 * HD)

    own_kv = to_units(key_values.reshape(HEADS * per_dev, tile_tokens, 2 * HD))
    anchored = to_units(
        jnp.broadcast_to(anchor_tile[:, None], key_values.shape).reshape(
            HEADS * per_dev, tile_tokens, 2 * HD
        )
    )

    other = lax.ppermute(own_kv, "core", [(0, 1), (1, 0)])
    pairs = []
    for v in range(views_n):
        for c in range(core_n):
            dest_view = (v + 1) % views_n if c == 1 else (v - 1) % views_n
            pairs.append((v * core_n + c, dest_view * core_n + (1 - c)))
    far = lax.ppermute(own_kv, ("view", "core"), pairs)
    nearby = jnp.where(
        slot == 1,
        jnp.concatenate([other, far], axis=0),
        jnp.concatenate([far, other], axis=0),
    )

    epi_rows = lax.dynamic_index_in_dim(epi_list, slot, 0, keepdims=False)
    epi_rows = lax.dynamic_slice_in_dim(epi_rows, half * (part_rows // BLK), part_rows // BLK, 0)
    attended = attention(epi_rows, q_mine, own_kv, anchored, nearby)
    attended = attended.reshape(half_n, tile_tokens, HD)
    returned = lax.all_to_all(attended, HALF, 0, 0, tiled=True)
    returned = returned.reshape(HEADS, per_dev, tile_tokens, HD)
    projected_out = jnp.einsum(
        "hvtc,hcd->vtd",
        returned,
        out_weight.reshape(HEADS, HD, model_width),
        preferred_element_type=jnp.float32,
    )
    return projected_out.astype(jnp.bfloat16)


def solution(mesh):
    views_n, tile_n = mesh.devices.shape
    fine = Mesh(
        mesh.devices.reshape(views_n, 2, tile_n // 8, 2, 2),
        ("view",) + SUB,
    )
    return jax.shard_map(
        body,
        mesh=fine,
        in_specs=(P("view", SUB, None), P(), P(), P(), P("view", None, None)),
        out_specs=P("view", SUB, None),
        check_vma=False,
    )
```

```python
import math

import jax
import jax.numpy as jnp
from jax import lax
from jax.experimental import pallas as pl
from jax.experimental.pallas import tpu as pltpu
from jax.sharding import Mesh
from jax.sharding import PartitionSpec as P

HEADS = 8
HD = 128
VT = 2048
BLK = 128
NBLK = 16

SUB = ("zh", "zl", "yhi", "core")
HALF = ("zl", "yhi", "core")


def attention_kernel(epi_ref, q_ref, own_ref, anc_ref, *rest):
    block = pl.program_id(0)
    nb_refs, o_ref = rest[:-1], rest[-1]
    queries = q_ref[...]
    scale = math.sqrt(HD)

    def scores_of(keyvals):
        return lax.dot_general(
            queries, keyvals[:, :HD], (((1,), (1,)), ((), ())),
            preferred_element_type=jnp.float32,
        ) / scale

    parts = []
    for ref in (own_ref, anc_ref):
        keyvals = ref[...]
        parts.append((scores_of(keyvals), keyvals))
    for slot, nb_ref in enumerate(nb_refs):
        index = epi_ref[block, slot]
        keyvals = nb_ref[...]
        scores = jnp.where(index >= 0, scores_of(keyvals), -jnp.inf)
        parts.append((scores, keyvals))
    peak = parts[0][0].max(axis=1, keepdims=True)
    for scores, _ in parts[1:]:
        peak = jnp.maximum(peak, scores.max(axis=1, keepdims=True))
    total = None
    summed = None
    for scores, keyvals in parts:
        raised = jnp.exp(scores - peak)
        row = raised.sum(axis=1, keepdims=True)
        prod = jnp.dot(raised.astype(jnp.bfloat16), keyvals[:, HD:], preferred_element_type=jnp.float32)
        total = row if total is None else total + row
        summed = prod if summed is None else summed + prod
    o_ref[...] = (summed / total).astype(o_ref.dtype)


def attention(epi_rows, queries, own, anchored, nearby):
    rows = queries.shape[0]
    spec_full = lambda n: pl.BlockSpec((n, 2 * HD), lambda b, epi: (0, 0))

    def spec_slot(slot):
        return pl.BlockSpec(
            (BLK, 2 * HD), lambda b, epi: (jnp.clip(epi[b, slot], 0, 2 * NBLK - 1), 0)
        )

    slots = epi_rows.shape[1]
    return pl.pallas_call(
        attention_kernel,
        out_shape=jax.ShapeDtypeStruct((rows, HD), jnp.bfloat16),
        grid_spec=pltpu.PrefetchScalarGridSpec(
            num_scalar_prefetch=1,
            grid=(rows // BLK,),
            in_specs=[
                pl.BlockSpec((BLK, HD), lambda b, epi: (b, 0)),
                spec_full(own.shape[0]),
                spec_full(anchored.shape[0]),
            ] + [spec_slot(e) for e in range(slots)],
            out_specs=pl.BlockSpec((BLK, HD), lambda b, epi: (b, 0)),
        ),
    )(epi_rows, queries, own, anchored, *([nearby] * slots))


def broadcast_view(value, root, count):
    me = lax.axis_index("view")
    dist = (me - root) % count
    held = jnp.where(dist == 0, value, jnp.zeros_like(value))
    reach = 0
    while 2 * reach + 1 < count:
        step = 2 * reach + 1
        up = lax.ppermute(held, "view", [(i, (i + step) % count) for i in range(count)])
        down = lax.ppermute(held, "view", [(i, (i - step) % count) for i in range(count)])
        lo = (dist >= reach + 1) & (dist <= reach + step)
        hi = (dist >= count - reach - step) & (dist <= count - reach - 1)
        held = jnp.where(lo, up, jnp.where(hi, down, held))
        reach += step
    return held


def body(latents, qkv_weight, out_weight, anchor, epi_list):
    per_dev, tile_tokens, model_width = latents.shape
    views_n = lax.axis_size("view")
    half_n = lax.axis_size(HALF)
    tile_n = lax.axis_size(SUB)
    part_rows = tile_tokens * half_n
    core_n = lax.axis_size("core")
    slot = lax.axis_index("core")
    half = lax.axis_index("zh")

    flat = jnp.dot(
        latents.reshape(per_dev * tile_tokens, model_width), qkv_weight,
        preferred_element_type=jnp.float32,
    ).astype(jnp.bfloat16)
    projected = flat.reshape(per_dev, tile_tokens, HEADS, 3 * HD).transpose(2, 0, 1, 3)
    key_values = projected[..., HD:]

    target = anchor[0]
    anchor_tile = lax.dynamic_index_in_dim(key_values, target % per_dev, 1, keepdims=False)
    anchor_tile = broadcast_view(anchor_tile, target // per_dev, views_n)

    def to_units(source):
        width = source.shape[-1]
        wide = jnp.broadcast_to(source[None], (tile_n // (HEADS * per_dev),) + source.shape)
        wide = wide.reshape(tile_n, tile_tokens, width)
        return lax.all_to_all(wide, SUB, 0, 0, tiled=True).reshape(tile_n * tile_tokens, width)

    resident = to_units(projected.reshape(HEADS * per_dev, tile_tokens, 3 * HD))
    q_mine = lax.dynamic_slice_in_dim(resident[:, :HD], half * part_rows, part_rows, 0)
    own_kv = resident[:, HD:]
    anchored = to_units(
        jnp.broadcast_to(anchor_tile[:, None], key_values.shape).reshape(
            HEADS * per_dev, tile_tokens, 2 * HD
        )
    )

    other = lax.ppermute(own_kv, "core", [(0, 1), (1, 0)])
    pairs = []
    for v in range(views_n):
        for c in range(core_n):
            dest_view = (v + 1) % views_n if c == 1 else (v - 1) % views_n
            pairs.append((v * core_n + c, dest_view * core_n + (1 - c)))
    far = lax.ppermute(own_kv, ("view", "core"), pairs)
    nearby = jnp.where(
        slot == 1,
        jnp.concatenate([other, far], axis=0),
        jnp.concatenate([far, other], axis=0),
    )

    epi_rows = lax.dynamic_index_in_dim(epi_list, slot, 0, keepdims=False)
    epi_rows = lax.dynamic_slice_in_dim(epi_rows, half * (part_rows // BLK), part_rows // BLK, 0)
    attended = attention(epi_rows, q_mine, own_kv, anchored, nearby)
    attended = attended.reshape(half_n, tile_tokens, HD)
    returned = lax.all_to_all(attended, HALF, 0, 0, tiled=True)
    returned = returned.reshape(HEADS, per_dev, tile_tokens, HD)
    projected_out = jnp.einsum(
        "hvtc,hcd->vtd",
        returned,
        out_weight.reshape(HEADS, HD, model_width),
        preferred_element_type=jnp.float32,
    )
    return projected_out.astype(jnp.bfloat16)


def solution(mesh):
    views_n, tile_n = mesh.devices.shape
    fine = Mesh(
        mesh.devices.reshape(views_n, 2, tile_n // 8, 2, 2),
        ("view",) + SUB,
    )
    return jax.shard_map(
        body,
        mesh=fine,
        in_specs=(P("view", SUB, None), P(), P(), P(), P("view", None, None)),
        out_specs=P("view", SUB, None),
        check_vma=False,
    )
```

```python
import math

import jax
import jax.numpy as jnp
from jax import lax
from jax.experimental import pallas as pl
from jax.experimental.pallas import tpu as pltpu
from jax.sharding import Mesh

from jax.sharding import PartitionSpec as P

HEADS = 8
HD = 128
BLK = 128
NBLK = 16

SUB = ("zh", "zl", "yhi", "core")
HALF = ("zl", "yhi", "core")


def attention_kernel(epi_ref, q_ref, own_ref, anc_ref, *rest):
    block = pl.program_id(0)
    nb_refs, o_ref = rest[:-1], rest[-1]
    queries = q_ref[...]
    scale = math.sqrt(HD)

    def scores_of(keyvals):
        return lax.dot_general(
            queries, keyvals[:, :HD], (((1,), (1,)), ((), ())),
            preferred_element_type=jnp.float32,
        ) / scale

    parts = []
    for ref in (own_ref, anc_ref):
        keyvals = ref[...]
        parts.append((scores_of(keyvals), keyvals))
    for slot, nb_ref in enumerate(nb_refs):
        index = epi_ref[block, slot]
        keyvals = nb_ref[...]
        scores = jnp.where(index >= 0, scores_of(keyvals), -jnp.inf)
        parts.append((scores, keyvals))
    peak = parts[0][0].max(axis=1, keepdims=True)
    for scores, _ in parts[1:]:
        peak = jnp.maximum(peak, scores.max(axis=1, keepdims=True))
    total = None
    summed = None
    for scores, keyvals in parts:
        raised = jnp.exp(scores - peak)
        row = raised.sum(axis=1, keepdims=True)
        prod = jnp.dot(raised.astype(jnp.bfloat16), keyvals[:, HD:], preferred_element_type=jnp.float32)
        total = row if total is None else total + row
        summed = prod if summed is None else summed + prod
    o_ref[...] = (summed / total).astype(o_ref.dtype)


def attention(epi_rows, queries, own, anchored, nearby):
    rows = queries.shape[0]
    spec_full = lambda n: pl.BlockSpec((n, 2 * HD), lambda b, epi: (0, 0))

    def spec_slot(slot):
        return pl.BlockSpec(
            (BLK, 2 * HD), lambda b, epi: (jnp.clip(epi[b, slot], 0, 2 * NBLK - 1), 0)
        )

    slots = epi_rows.shape[1]
    return pl.pallas_call(
        attention_kernel,
        out_shape=jax.ShapeDtypeStruct((rows, HD), jnp.bfloat16),
        grid_spec=pltpu.PrefetchScalarGridSpec(
            num_scalar_prefetch=1,
            grid=(rows // BLK,),
            in_specs=[
                pl.BlockSpec((BLK, HD), lambda b, epi: (b, 0)),
                spec_full(own.shape[0]),
                spec_full(anchored.shape[0]),
            ] + [spec_slot(e) for e in range(slots)],
            out_specs=pl.BlockSpec((BLK, HD), lambda b, epi: (b, 0)),
        ),
    )(epi_rows, queries, own, anchored, *([nearby] * slots))


def broadcast_view(value, root, count):
    me = lax.axis_index("view")
    dist = (me - root) % count
    held = jnp.where(dist == 0, value, jnp.zeros_like(value))
    reach = 0
    while 2 * reach + 1 < count:
        step = 2 * reach + 1
        up = lax.ppermute(held, "view", [(i, (i + step) % count) for i in range(count)])
        down = lax.ppermute(held, "view", [(i, (i - step) % count) for i in range(count)])
        lo = (dist >= reach + 1) & (dist <= reach + step)
        hi = (dist >= count - reach - step) & (dist <= count - reach - 1)
        held = jnp.where(lo, up, jnp.where(hi, down, held))
        reach += step
    return held


def layer(latents, qkv_weight, out_weight, anchor, epi_list):
    per_dev, tile_tokens, model_width = latents.shape
    views_n = lax.axis_size("view")
    half_n = lax.axis_size(HALF)
    tile_n = lax.axis_size(SUB)
    part_rows = tile_tokens * half_n
    core_n = lax.axis_size("core")
    slot = lax.axis_index("core")
    half = lax.axis_index("zh")

    target = anchor[0]
    anchor_latents = lax.dynamic_index_in_dim(latents, target % per_dev, 0, keepdims=False)
    anchor_latents = broadcast_view(anchor_latents, target // per_dev, views_n)

    flat = jnp.dot(
        latents.reshape(per_dev * tile_tokens, model_width), qkv_weight,
        preferred_element_type=jnp.float32,
    ).astype(jnp.bfloat16)
    projected = flat.reshape(per_dev, tile_tokens, HEADS, 3 * HD).transpose(2, 0, 1, 3)
    key_values = projected[..., HD:]

    anchor_tile = jnp.dot(
        anchor_latents, qkv_weight, preferred_element_type=jnp.float32
    ).astype(jnp.bfloat16)
    anchor_tile = anchor_tile.reshape(tile_tokens, HEADS, 3 * HD)[..., HD:].transpose(1, 0, 2)

    def to_units(source):
        width = source.shape[-1]
        wide = jnp.broadcast_to(source[None], (tile_n // (HEADS * per_dev),) + source.shape)
        wide = wide.reshape(tile_n, tile_tokens, width)
        return lax.all_to_all(wide, SUB, 0, 0, tiled=True).reshape(tile_n * tile_tokens, width)

    resident = to_units(projected.reshape(HEADS * per_dev, tile_tokens, 3 * HD))
    q_mine = lax.dynamic_slice_in_dim(resident[:, :HD], half * part_rows, part_rows, 0)
    own_kv = resident[:, HD:]
    anchored = to_units(
        jnp.broadcast_to(anchor_tile[:, None], key_values.shape).reshape(
            HEADS * per_dev, tile_tokens, 2 * HD
        )
    )

    other = lax.ppermute(own_kv, "core", [(0, 1), (1, 0)])
    pairs = []
    for v in range(views_n):
        for c in range(core_n):
            dest_view = (v + 1) % views_n if c == 1 else (v - 1) % views_n
            pairs.append((v * core_n + c, dest_view * core_n + (1 - c)))
    far = lax.ppermute(own_kv, ("view", "core"), pairs)
    nearby = jnp.where(
        slot == 1,
        jnp.concatenate([other, far], axis=0),
        jnp.concatenate([far, other], axis=0),
    )

    epi_rows = lax.dynamic_index_in_dim(epi_list, slot, 0, keepdims=False)
    epi_rows = lax.dynamic_slice_in_dim(epi_rows, half * (part_rows // BLK), part_rows // BLK, 0)
    attended = attention(epi_rows, q_mine, own_kv, anchored, nearby)
    attended = attended.reshape(half_n, tile_tokens, HD)
    returned = lax.all_to_all(attended, HALF, 0, 0, tiled=True)
    returned = returned.reshape(HEADS, per_dev, tile_tokens, HD)
    projected_out = jnp.einsum(
        "hvtc,hcd->vtd",
        returned,
        out_weight.reshape(HEADS, HD, model_width),
        preferred_element_type=jnp.float32,
    )
    return projected_out.astype(jnp.bfloat16)


def solution(mesh):
    views_n, tile_n = mesh.devices.shape
    fine = Mesh(
        mesh.devices.reshape(views_n, 2, tile_n // 8, 2, 2),
        ("view",) + SUB,
    )
    return jax.shard_map(
        layer,
        mesh=fine,
        in_specs=(P("view", SUB, None), P(), P(), P(), P("view", None, None)),
        out_specs=P("view", SUB, None),
        check_vma=False,
    )
```

```python
import math

import jax
import jax.numpy as jnp
from jax import lax
from jax.experimental import pallas as pl
from jax.experimental.pallas import tpu as pltpu
from jax.sharding import Mesh

from jax.sharding import PartitionSpec as P

HEADS = 8
HD = 128
BLK = 128
NBLK = 16

SUB = ("zh", "zl", "yhi", "core")
HALF = ("zl", "yhi", "core")


def attention_kernel(epi_ref, flag_ref, q_ref, own_ref, anc_ref, *rest):
    block = pl.program_id(0)
    slots = epi_ref.shape[1]
    other_refs, far_refs, o_ref = rest[:slots], rest[slots:-1], rest[-1]
    queries = q_ref[...]
    scale = math.sqrt(HD)

    def scores_of(keys):
        return lax.dot_general(
            queries, keys, (((1,), (1,)), ((), ())),
            preferred_element_type=jnp.float32,
        ) / scale

    own = own_ref[...]
    anc = anc_ref[...]
    parts = [
        (scores_of(own[:, HD : 2 * HD]), own[:, 2 * HD :]),
        (scores_of(anc[:, :HD]), anc[:, HD:]),
    ]
    for slot in range(slots):
        index = epi_ref[block, slot]
        use_other = (index < NBLK) == (flag_ref[0] == 1)
        keyvals = jnp.where(use_other, other_refs[slot][...], far_refs[slot][...])
        scores = jnp.where(index >= 0, scores_of(keyvals[:, :HD]), -jnp.inf)
        parts.append((scores, keyvals[:, HD:]))
    peak = parts[0][0].max(axis=1, keepdims=True)
    for scores, _ in parts[1:]:
        peak = jnp.maximum(peak, scores.max(axis=1, keepdims=True))
    total = None
    summed = None
    for scores, values in parts:
        raised = jnp.exp(scores - peak)
        row = raised.sum(axis=1, keepdims=True)
        prod = jnp.dot(raised.astype(jnp.bfloat16), values, preferred_element_type=jnp.float32)
        total = row if total is None else total + row
        summed = prod if summed is None else summed + prod
    o_ref[...] = (summed / total).astype(o_ref.dtype)


def attention(epi_rows, flags, resident, anchored, other, far, rows):
    slots = epi_rows.shape[1]

    def spec_slot(slot):
        return pl.BlockSpec(
            (BLK, 2 * HD),
            lambda b, epi, flag: (jnp.clip(epi[b, slot], 0, 2 * NBLK - 1) % NBLK, 0),
        )

    return pl.pallas_call(
        attention_kernel,
        out_shape=jax.ShapeDtypeStruct((rows, HD), jnp.bfloat16),
        grid_spec=pltpu.PrefetchScalarGridSpec(
            num_scalar_prefetch=2,
            grid=(rows // BLK,),
            in_specs=[
                pl.BlockSpec((BLK, HD), lambda b, epi, flag: (flag[1] + b, 0)),
                pl.BlockSpec(resident.shape, lambda b, epi, flag: (0, 0)),
                pl.BlockSpec(anchored.shape, lambda b, epi, flag: (0, 0)),
            ]
            + [spec_slot(e) for e in range(slots)]
            + [spec_slot(e) for e in range(slots)],
            out_specs=pl.BlockSpec((BLK, HD), lambda b, epi, flag: (b, 0)),
        ),
    )(epi_rows, flags, resident, resident, anchored, *([other] * slots), *([far] * slots))


def broadcast_view(value, root, count):
    me = lax.axis_index("view")
    dist = (me - root) % count
    held = jnp.where(dist == 0, value, jnp.zeros_like(value))
    reach = 0
    while 2 * reach + 1 < count:
        step = 2 * reach + 1
        up = lax.ppermute(held, "view", [(i, (i + step) % count) for i in range(count)])
        down = lax.ppermute(held, "view", [(i, (i - step) % count) for i in range(count)])
        lo = (dist >= reach + 1) & (dist <= reach + step)
        hi = (dist >= count - reach - step) & (dist <= count - reach - 1)
        held = jnp.where(lo, up, jnp.where(hi, down, held))
        reach += step
    return held


def layer(latents, qkv_weight, out_weight, anchor, epi_list):
    per_dev, tile_tokens, model_width = latents.shape
    views_n = lax.axis_size("view")
    half_n = lax.axis_size(HALF)
    tile_n = lax.axis_size(SUB)
    part_rows = tile_tokens * half_n
    core_n = lax.axis_size("core")
    slot = lax.axis_index("core")
    half = lax.axis_index("zh")

    target = anchor[0]
    anchor_latents = lax.dynamic_index_in_dim(latents, target % per_dev, 0, keepdims=False)
    anchor_latents = broadcast_view(anchor_latents, target // per_dev, views_n)

    flat = jnp.dot(
        latents.reshape(per_dev * tile_tokens, model_width), qkv_weight,
        preferred_element_type=jnp.float32,
    ).astype(jnp.bfloat16)
    projected = flat.reshape(per_dev, tile_tokens, HEADS, 3 * HD).transpose(2, 0, 1, 3)
    key_values = projected[..., HD:]

    anchor_tile = jnp.dot(
        anchor_latents, qkv_weight, preferred_element_type=jnp.float32
    ).astype(jnp.bfloat16)
    anchor_tile = anchor_tile.reshape(tile_tokens, HEADS, 3 * HD)[..., HD:].transpose(1, 0, 2)

    def to_units(source):
        width = source.shape[-1]
        wide = jnp.broadcast_to(source[None], (tile_n // (HEADS * per_dev),) + source.shape)
        wide = wide.reshape(tile_n, tile_tokens, width)
        return lax.all_to_all(wide, SUB, 0, 0, tiled=True).reshape(tile_n * tile_tokens, width)

    resident = to_units(projected.reshape(HEADS * per_dev, tile_tokens, 3 * HD))
    own_kv = resident[:, HD:]
    anchored = to_units(
        jnp.broadcast_to(anchor_tile[:, None], key_values.shape).reshape(
            HEADS * per_dev, tile_tokens, 2 * HD
        )
    )

    other = lax.ppermute(own_kv, "core", [(0, 1), (1, 0)])
    pairs = []
    for v in range(views_n):
        for c in range(core_n):
            dest_view = (v + 1) % views_n if c == 1 else (v - 1) % views_n
            pairs.append((v * core_n + c, dest_view * core_n + (1 - c)))
    far = lax.ppermute(own_kv, ("view", "core"), pairs)
    epi_rows = lax.dynamic_index_in_dim(epi_list, slot, 0, keepdims=False)
    epi_rows = lax.dynamic_slice_in_dim(epi_rows, half * (part_rows // BLK), part_rows // BLK, 0)
    flags = jnp.stack([slot, half * (part_rows // BLK)]).astype(jnp.int32)
    attended = attention(epi_rows, flags, resident, anchored, other, far, part_rows)
    attended = attended.reshape(half_n, tile_tokens, HD)
    returned = lax.all_to_all(attended, HALF, 0, 0, tiled=True)
    returned = returned.reshape(HEADS, per_dev, tile_tokens, HD)
    projected_out = jnp.einsum(
        "hvtc,hcd->vtd",
        returned,
        out_weight.reshape(HEADS, HD, model_width),
        preferred_element_type=jnp.float32,
    )
    return projected_out.astype(jnp.bfloat16)


def solution(mesh):
    views_n, tile_n = mesh.devices.shape
    fine = Mesh(
        mesh.devices.reshape(views_n, 2, tile_n // 8, 2, 2),
        ("view",) + SUB,
    )
    return jax.shard_map(
        layer,
        mesh=fine,
        in_specs=(P("view", SUB, None), P(), P(), P(), P("view", None, None)),
        out_specs=P("view", SUB, None),
        check_vma=False,
    )
```

```python
import math

import jax
import jax.numpy as jnp
from jax import lax
from jax.experimental import pallas as pl
from jax.experimental.pallas import tpu as pltpu
from jax.sharding import Mesh

from jax.sharding import PartitionSpec as P

HEADS = 8
HD = 128
BLK = 128
NBLK = 16

SUB = ("zh", "zl", "yhi", "core")
CHIPS = ("zh", "zl", "yhi")


def attention_kernel(epi_ref, flag_ref, q_ref, own_ref, anc_ref, *rest):
    block = pl.program_id(0)
    slots = epi_ref.shape[1]
    other_refs, far_refs, o_ref = rest[:slots], rest[slots:-1], rest[-1]
    queries = q_ref[...]
    scale = math.sqrt(HD)

    def scores_of(keys):
        return lax.dot_general(
            queries, keys, (((1,), (1,)), ((), ())),
            preferred_element_type=jnp.float32,
        ) / scale

    own = own_ref[...]
    anc = anc_ref[...]
    parts = [
        (scores_of(own[:, :HD]), own[:, HD:]),
        (scores_of(anc[:, :HD]), anc[:, HD:]),
    ]
    for slot in range(slots):
        index = epi_ref[block, slot]
        use_other = (index < NBLK) == (flag_ref[0] == 1)
        keyvals = jnp.where(use_other, other_refs[slot][...], far_refs[slot][...])
        scores = jnp.where(index >= 0, scores_of(keyvals[:, :HD]), -jnp.inf)
        parts.append((scores, keyvals[:, HD:]))
    peak = parts[0][0].max(axis=1, keepdims=True)
    for scores, _ in parts[1:]:
        peak = jnp.maximum(peak, scores.max(axis=1, keepdims=True))
    total = None
    summed = None
    for scores, values in parts:
        raised = jnp.exp(scores - peak)
        row = raised.sum(axis=1, keepdims=True)
        prod = jnp.dot(raised.astype(jnp.bfloat16), values, preferred_element_type=jnp.float32)
        total = row if total is None else total + row
        summed = prod if summed is None else summed + prod
    o_ref[...] = (summed / total).astype(o_ref.dtype)


def attention(epi_rows, flags, resident, own, anchored, other, far, q_rows):
    slots = epi_rows.shape[1]
    blocks = epi_rows.shape[0]
    parts = BLK // q_rows

    def spec_slot(slot):
        return pl.BlockSpec(
            (BLK, 2 * HD),
            lambda b, epi, flag: (jnp.clip(epi[b, slot], 0, 2 * NBLK - 1) % NBLK, 0),
        )

    return pl.pallas_call(
        attention_kernel,
        out_shape=jax.ShapeDtypeStruct((blocks * q_rows, HD), jnp.bfloat16),
        grid_spec=pltpu.PrefetchScalarGridSpec(
            num_scalar_prefetch=2,
            grid=(blocks,),
            in_specs=[
                pl.BlockSpec((q_rows, HD), lambda b, epi, flag: (parts * b + flag[1], 0)),
                pl.BlockSpec(own.shape, lambda b, epi, flag: (0, 0)),
                pl.BlockSpec(anchored.shape, lambda b, epi, flag: (0, 0)),
            ]
            + [spec_slot(e) for e in range(slots)]
            + [spec_slot(e) for e in range(slots)],
            out_specs=pl.BlockSpec((q_rows, HD), lambda b, epi, flag: (b, 0)),
        ),
    )(epi_rows, flags, resident, own, anchored, *([other] * slots), *([far] * slots))


def broadcast_view(value, root, count):
    me = lax.axis_index("view")
    dist = (me - root) % count
    held = jnp.where(dist == 0, value, jnp.zeros_like(value))
    reach = 0
    while 2 * reach + 1 < count:
        step = 2 * reach + 1
        up = lax.ppermute(held, "view", [(i, (i + step) % count) for i in range(count)])
        down = lax.ppermute(held, "view", [(i, (i - step) % count) for i in range(count)])
        lo = (dist >= reach + 1) & (dist <= reach + step)
        hi = (dist >= count - reach - step) & (dist <= count - reach - 1)
        held = jnp.where(lo, up, jnp.where(hi, down, held))
        reach += step
    return held


def layer(latents, qkv_weight, out_weight, anchor, epi_list):
    per_dev, tile_tokens, model_width = latents.shape
    views_n = lax.axis_size("view")
    tile_n = lax.axis_size(SUB)
    zl_n = lax.axis_size("zl")
    part = lax.axis_index("core")
    slot = lax.axis_index("zl") % 2

    target = anchor[0]
    anchor_latents = lax.dynamic_index_in_dim(latents, target % per_dev, 0, keepdims=False)
    anchor_latents = broadcast_view(anchor_latents, target // per_dev, views_n)

    flat = jnp.dot(
        latents.reshape(per_dev * tile_tokens, model_width), qkv_weight,
        preferred_element_type=jnp.float32,
    ).astype(jnp.bfloat16)
    projected = flat.reshape(per_dev, tile_tokens, HEADS, 3 * HD).transpose(2, 0, 1, 3)

    anchor_tile = jnp.dot(
        anchor_latents, qkv_weight, preferred_element_type=jnp.float32
    ).astype(jnp.bfloat16)
    anchor_tile = anchor_tile.reshape(tile_tokens, HEADS, 3 * HD)[..., HD:].transpose(1, 0, 2)

    by_unit = projected.reshape(2, 2, 2, per_dev, tile_tokens, 3 * HD).transpose(0, 1, 3, 2, 4, 5)
    anchor_by = jnp.broadcast_to(
        anchor_tile.reshape(2, 2, 1, 2, tile_tokens, 2 * HD), by_unit.shape[:-1] + (2 * HD,)
    )
    with_anchor = jnp.concatenate([by_unit[..., :HD], anchor_by], axis=-1)
    send = jnp.stack([by_unit, with_anchor], axis=4).reshape(tile_n, tile_tokens, 3 * HD)
    received = lax.all_to_all(send, SUB, 0, 0, tiled=True).reshape(tile_n * tile_tokens, 3 * HD)
    mine = received[:, HD:]
    swapped = lax.ppermute(mine, "core", [(0, 1), (1, 0)])
    own_kv = jnp.where(part == 0, mine, swapped)
    anchored = jnp.where(part == 0, swapped, mine)

    other = lax.ppermute(own_kv, "zl", [(z, z ^ 1) for z in range(zl_n)])
    pairs = []
    for v in range(views_n):
        for z in range(zl_n):
            dest_view = (v + 1) % views_n if z % 2 == 1 else (v - 1) % views_n
            pairs.append((v * zl_n + z, dest_view * zl_n + (z ^ 1)))
    far = lax.ppermute(own_kv, ("view", "zl"), pairs)

    epi_rows = lax.dynamic_index_in_dim(epi_list, slot, 0, keepdims=False)
    flags = jnp.stack([slot, part]).astype(jnp.int32)
    attended = attention(epi_rows, flags, received, own_kv, anchored, other, far, tile_tokens)
    chips_n = tile_n // 2
    attended = attended.reshape(chips_n, tile_tokens, HD)
    returned = lax.all_to_all(attended, CHIPS, 0, 0, tiled=True)
    returned = returned.reshape(2, 2, per_dev, 2, tile_tokens, HD).transpose(0, 1, 3, 2, 4, 5)
    returned = returned.reshape(HEADS, per_dev, tile_tokens, HD)
    projected_out = jnp.einsum(
        "hvtc,hcd->vtd",
        returned,
        out_weight.reshape(HEADS, HD, model_width),
        preferred_element_type=jnp.float32,
    )
    return projected_out.astype(jnp.bfloat16)


def solution(mesh):
    views_n, tile_n = mesh.devices.shape
    fine = Mesh(
        mesh.devices.reshape(views_n, 2, tile_n // 8, 2, 2),
        ("view",) + SUB,
    )
    return jax.shard_map(
        layer,
        mesh=fine,
        in_specs=(P("view", SUB, None), P(), P(), P(), P("view", None, None)),
        out_specs=P("view", SUB, None),
        check_vma=False,
    )
```

```python
import math

import jax
import jax.numpy as jnp
from jax import lax
from jax.experimental import pallas as pl
from jax.experimental.pallas import tpu as pltpu
from jax.sharding import Mesh

from jax.sharding import PartitionSpec as P

HEADS = 8
HD = 128
BLK = 128
NBLK = 16

SUB = ("zh", "zl", "yhi", "core")
HALF = ("zl", "yhi", "core")


def attention_kernel(epi_ref, flag_ref, q_ref, own_ref, anc_ref, anc2_ref, *rest):
    block = pl.program_id(0)
    slots = epi_ref.shape[1]
    other_refs, far_refs, o_ref = rest[:slots], rest[slots:-1], rest[-1]
    queries = q_ref[...]
    scale = math.sqrt(HD)

    def scores_of(keys):
        return lax.dot_general(
            queries, keys, (((1,), (1,)), ((), ())),
            preferred_element_type=jnp.float32,
        ) / scale

    own = own_ref[...]
    anc = anc_ref[...]
    anc2 = anc2_ref[...]
    parts = [
        (scores_of(own[:, HD : 2 * HD]), own[:, 2 * HD :]),
        (scores_of(anc[:, :HD]), anc[:, HD:]),
        (scores_of(anc2[:, :HD]), anc2[:, HD:]),
    ]
    for slot in range(slots):
        index = epi_ref[block, slot]
        use_other = (index < NBLK) == (flag_ref[0] == 1)
        keyvals = jnp.where(use_other, other_refs[slot][...], far_refs[slot][...])
        scores = jnp.where(index >= 0, scores_of(keyvals[:, :HD]), -jnp.inf)
        parts.append((scores, keyvals[:, HD:]))
    peak = parts[0][0].max(axis=1, keepdims=True)
    for scores, _ in parts[1:]:
        peak = jnp.maximum(peak, scores.max(axis=1, keepdims=True))
    total = None
    summed = None
    for scores, values in parts:
        raised = jnp.exp(scores - peak)
        row = raised.sum(axis=1, keepdims=True)
        prod = jnp.dot(raised.astype(jnp.bfloat16), values, preferred_element_type=jnp.float32)
        total = row if total is None else total + row
        summed = prod if summed is None else summed + prod
    o_ref[...] = (summed / total).astype(o_ref.dtype)


def attention(epi_rows, flags, resident, anchored, anchored2, other, far, rows):
    slots = epi_rows.shape[1]

    def spec_slot(slot, want_other):
        def index_map(b, epi, flag):
            index = epi[b, slot]
            used = (index >= 0) & ((index < NBLK) == ((flag[0] == 1) == want_other))
            return (jnp.where(used, jnp.clip(index, 0, 2 * NBLK - 1) % NBLK, 0), 0)

        return pl.BlockSpec((BLK, 2 * HD), index_map)

    return pl.pallas_call(
        attention_kernel,
        out_shape=jax.ShapeDtypeStruct((rows, HD), jnp.bfloat16),
        grid_spec=pltpu.PrefetchScalarGridSpec(
            num_scalar_prefetch=2,
            grid=(rows // BLK,),
            in_specs=[
                pl.BlockSpec((BLK, HD), lambda b, epi, flag: (flag[1] + b, 0)),
                pl.BlockSpec(resident.shape, lambda b, epi, flag: (0, 0)),
                pl.BlockSpec(anchored.shape, lambda b, epi, flag: (0, 0)),
                pl.BlockSpec(anchored2.shape, lambda b, epi, flag: (0, 0)),
            ]
            + [spec_slot(e, True) for e in range(slots)]
            + [spec_slot(e, False) for e in range(slots)],
            out_specs=pl.BlockSpec((BLK, HD), lambda b, epi, flag: (b, 0)),
        ),
    )(epi_rows, flags, resident, resident, anchored, anchored2, *([other] * slots), *([far] * slots))


def broadcast_view(value, root, count):
    me = lax.axis_index("view")
    dist = (me - root) % count
    held = jnp.where(dist == 0, value, jnp.zeros_like(value))
    reach = 0
    while 2 * reach + 1 < count:
        step = 2 * reach + 1
        up = lax.ppermute(held, "view", [(i, (i + step) % count) for i in range(count)])
        down = lax.ppermute(held, "view", [(i, (i - step) % count) for i in range(count)])
        lo = (dist >= reach + 1) & (dist <= reach + step)
        hi = (dist >= count - reach - step) & (dist <= count - reach - 1)
        held = jnp.where(lo, up, jnp.where(hi, down, held))
        reach += step
    return held


def layer(latents, qkv_weight, out_weight, anchor, epi_list):
    per_dev, tile_tokens, model_width = latents.shape
    views_n = lax.axis_size("view")
    half_n = lax.axis_size(HALF)
    tile_n = lax.axis_size(SUB)
    part_rows = tile_tokens * half_n
    core_n = lax.axis_size("core")
    slot = lax.axis_index("core")
    half = lax.axis_index("zh")

    target = anchor[0]
    anchor_latents = lax.dynamic_index_in_dim(latents, target % per_dev, 0, keepdims=False)
    anchor_latents = broadcast_view(anchor_latents, target // per_dev, views_n)

    flat = jnp.dot(
        latents.reshape(per_dev * tile_tokens, model_width), qkv_weight,
        preferred_element_type=jnp.float32,
    ).astype(jnp.bfloat16)
    projected = flat.reshape(per_dev, tile_tokens, HEADS, 3 * HD).transpose(2, 0, 1, 3)

    anchor_tile = jnp.dot(
        anchor_latents, qkv_weight, preferred_element_type=jnp.float32
    ).astype(jnp.bfloat16)
    anchor_tile = anchor_tile.reshape(tile_tokens, HEADS, 3 * HD)[..., HD:].transpose(1, 0, 2)

    def to_units(source):
        width = source.shape[-1]
        wide = jnp.broadcast_to(source[None], (tile_n // (HEADS * per_dev),) + source.shape)
        wide = wide.reshape(tile_n, tile_tokens, width)
        return lax.all_to_all(wide, SUB, 0, 0, tiled=True).reshape(tile_n * tile_tokens, width)

    resident = to_units(projected.reshape(HEADS * per_dev, tile_tokens, 3 * HD))
    own_kv = resident[:, HD:]
    halves = anchor_tile.reshape(HEADS * core_n, tile_tokens // core_n, 2 * HD)
    wide = jnp.broadcast_to(halves[None], (tile_n // (HEADS * core_n),) + halves.shape)
    wide = wide.reshape(tile_n, tile_tokens // core_n, 2 * HD)
    anchored = lax.all_to_all(wide, SUB, 0, 0, tiled=True).reshape(-1, 2 * HD)
    anchored2 = lax.ppermute(anchored, "core", [(0, 1), (1, 0)])

    other = lax.ppermute(own_kv, "core", [(0, 1), (1, 0)])
    pairs = []
    for v in range(views_n):
        for c in range(core_n):
            dest_view = (v + 1) % views_n if c == 1 else (v - 1) % views_n
            pairs.append((v * core_n + c, dest_view * core_n + (1 - c)))
    far = lax.ppermute(own_kv, ("view", "core"), pairs)
    epi_rows = lax.dynamic_index_in_dim(epi_list, slot, 0, keepdims=False)
    epi_rows = lax.dynamic_slice_in_dim(epi_rows, half * (part_rows // BLK), part_rows // BLK, 0)
    flags = jnp.stack([slot, half * (part_rows // BLK)]).astype(jnp.int32)
    attended = attention(epi_rows, flags, resident, anchored, anchored2, other, far, part_rows)
    attended = attended.reshape(half_n, tile_tokens, HD)
    returned = lax.all_to_all(attended, HALF, 0, 0, tiled=True)
    returned = returned.reshape(HEADS, per_dev, tile_tokens, HD)
    projected_out = jnp.einsum(
        "hvtc,hcd->vtd",
        returned,
        out_weight.reshape(HEADS, HD, model_width),
        preferred_element_type=jnp.float32,
    )
    return projected_out.astype(jnp.bfloat16)


def solution(mesh):
    views_n, tile_n = mesh.devices.shape
    fine = Mesh(
        mesh.devices.reshape(views_n, 2, tile_n // 8, 2, 2),
        ("view",) + SUB,
    )
    return jax.shard_map(
        layer,
        mesh=fine,
        in_specs=(P("view", SUB, None), P(), P(), P(), P("view", None, None)),
        out_specs=P("view", SUB, None),
        check_vma=False,
    )
```

```python
import math

import jax
import jax.numpy as jnp
from jax import lax
from jax.experimental import pallas as pl
from jax.experimental.pallas import tpu as pltpu
from jax.sharding import Mesh

from jax.sharding import PartitionSpec as P

HEADS = 8
HD = 128
BLK = 128
NBLK = 16

SUB = ("zh", "zl", "yhi", "core")
HALF = ("zl", "yhi", "core")


def attention_kernel(epi_ref, flag_ref, q_ref, own_ref, anc_ref, anc2_ref, *rest):
    block = pl.program_id(0)
    slots = epi_ref.shape[1]
    other_refs, far_refs, o_ref = rest[:slots], rest[slots:-1], rest[-1]
    queries = q_ref[...]
    inverse = 1.0 / math.sqrt(HD)

    def scores_of(keys):
        return lax.dot_general(
            queries, keys, (((1,), (1,)), ((), ())),
            preferred_element_type=jnp.float32,
        ) * inverse

    own = own_ref[...]
    anc = anc_ref[...]
    anc2 = anc2_ref[...]
    parts = [
        (scores_of(own[:, HD : 2 * HD]), own[:, 2 * HD :]),
        (scores_of(anc[:, :HD]), anc[:, HD:]),
        (scores_of(anc2[:, :HD]), anc2[:, HD:]),
    ]
    for slot in range(slots):
        index = epi_ref[block, slot]
        use_other = (index < NBLK) == (flag_ref[0] == 1)
        keyvals = jnp.where(use_other, other_refs[slot][...], far_refs[slot][...])
        scores = jnp.where(index >= 0, scores_of(keyvals[:, :HD]), -jnp.inf)
        parts.append((scores, keyvals[:, HD:]))
    peak = parts[0][0].max(axis=1, keepdims=True)
    for scores, _ in parts[1:]:
        peak = jnp.maximum(peak, scores.max(axis=1, keepdims=True))
    total = None
    summed = None
    for scores, values in parts:
        raised = jnp.exp(scores - peak)
        row = raised.sum(axis=1, keepdims=True)
        prod = jnp.dot(raised.astype(jnp.bfloat16), values, preferred_element_type=jnp.float32)
        total = row if total is None else total + row
        summed = prod if summed is None else summed + prod
    o_ref[...] = (summed / total).astype(o_ref.dtype)


def attention(epi_rows, flags, resident, anchored, anchored2, other, far, rows):
    slots = epi_rows.shape[1]

    def spec_slot(slot):
        return pl.BlockSpec(
            (BLK, 2 * HD),
            lambda b, epi, flag: (jnp.clip(epi[b, slot], 0, 2 * NBLK - 1) % NBLK, 0),
        )

    return pl.pallas_call(
        attention_kernel,
        out_shape=jax.ShapeDtypeStruct((rows, HD), jnp.bfloat16),
        grid_spec=pltpu.PrefetchScalarGridSpec(
            num_scalar_prefetch=2,
            grid=(rows // BLK,),
            in_specs=[
                pl.BlockSpec((BLK, HD), lambda b, epi, flag: (flag[1] + b, 0)),
                pl.BlockSpec(resident.shape, lambda b, epi, flag: (0, 0)),
                pl.BlockSpec(anchored.shape, lambda b, epi, flag: (0, 0)),
                pl.BlockSpec(anchored2.shape, lambda b, epi, flag: (0, 0)),
            ]
            + [spec_slot(e) for e in range(slots)]
            + [spec_slot(e) for e in range(slots)],
            out_specs=pl.BlockSpec((BLK, HD), lambda b, epi, flag: (b, 0)),
        ),
    )(epi_rows, flags, resident, resident, anchored, anchored2, *([other] * slots), *([far] * slots))


def broadcast_view(value, root, count):
    me = lax.axis_index("view")
    dist = (me - root) % count
    held = jnp.where(dist == 0, value, jnp.zeros_like(value))
    reach = 0
    while 2 * reach + 1 < count:
        step = 2 * reach + 1
        up = lax.ppermute(held, "view", [(i, (i + step) % count) for i in range(count)])
        down = lax.ppermute(held, "view", [(i, (i - step) % count) for i in range(count)])
        lo = (dist >= reach + 1) & (dist <= reach + step)
        hi = (dist >= count - reach - step) & (dist <= count - reach - 1)
        held = jnp.where(lo, up, jnp.where(hi, down, held))
        reach += step
    return held


def layer(latents, qkv_weight, out_weight, anchor, epi_list):
    per_dev, tile_tokens, model_width = latents.shape
    views_n = lax.axis_size("view")
    half_n = lax.axis_size(HALF)
    tile_n = lax.axis_size(SUB)
    part_rows = tile_tokens * half_n
    core_n = lax.axis_size("core")
    slot = lax.axis_index("core")
    half = lax.axis_index("zh")

    target = anchor[0]
    anchor_latents = lax.dynamic_index_in_dim(latents, target % per_dev, 0, keepdims=False)
    anchor_latents = broadcast_view(anchor_latents, target // per_dev, views_n)

    flat = jnp.dot(
        latents.reshape(per_dev * tile_tokens, model_width), qkv_weight,
        preferred_element_type=jnp.float32,
    ).astype(jnp.bfloat16)
    projected = flat.reshape(per_dev, tile_tokens, HEADS, 3 * HD).transpose(2, 0, 1, 3)

    anchor_tile = jnp.dot(
        anchor_latents, qkv_weight, preferred_element_type=jnp.float32
    ).astype(jnp.bfloat16)
    anchor_tile = anchor_tile.reshape(tile_tokens, HEADS, 3 * HD)[..., HD:].transpose(1, 0, 2)

    def to_units(source):
        width = source.shape[-1]
        wide = jnp.broadcast_to(source[None], (tile_n // (HEADS * per_dev),) + source.shape)
        wide = wide.reshape(tile_n, tile_tokens, width)
        return lax.all_to_all(wide, SUB, 0, 0, tiled=True).reshape(tile_n * tile_tokens, width)

    resident = to_units(projected.reshape(HEADS * per_dev, tile_tokens, 3 * HD))
    own_kv = resident[:, HD:]
    halves = anchor_tile.reshape(HEADS * core_n, tile_tokens // core_n, 2 * HD)
    wide = jnp.broadcast_to(halves[None], (tile_n // (HEADS * core_n),) + halves.shape)
    wide = wide.reshape(tile_n, tile_tokens // core_n, 2 * HD)
    anchored = lax.all_to_all(wide, SUB, 0, 0, tiled=True).reshape(-1, 2 * HD)
    anchored2 = lax.ppermute(anchored, "core", [(0, 1), (1, 0)])

    other = lax.ppermute(own_kv, "core", [(0, 1), (1, 0)])
    pairs = []
    for v in range(views_n):
        for c in range(core_n):
            dest_view = (v + 1) % views_n if c == 1 else (v - 1) % views_n
            pairs.append((v * core_n + c, dest_view * core_n + (1 - c)))
    far = lax.ppermute(own_kv, ("view", "core"), pairs)
    epi_rows = lax.dynamic_index_in_dim(epi_list, slot, 0, keepdims=False)
    epi_rows = lax.dynamic_slice_in_dim(epi_rows, half * (part_rows // BLK), part_rows // BLK, 0)
    flags = jnp.stack([slot, half * (part_rows // BLK)]).astype(jnp.int32)
    attended = attention(epi_rows, flags, resident, anchored, anchored2, other, far, part_rows)
    attended = attended.reshape(half_n, tile_tokens, HD)
    returned = lax.all_to_all(attended, HALF, 0, 0, tiled=True)
    returned = returned.reshape(HEADS, per_dev, tile_tokens, HD)
    projected_out = jnp.einsum(
        "hvtc,hcd->vtd",
        returned,
        out_weight.reshape(HEADS, HD, model_width),
        preferred_element_type=jnp.float32,
    )
    return projected_out.astype(jnp.bfloat16)


def solution(mesh):
    views_n, tile_n = mesh.devices.shape
    fine = Mesh(
        mesh.devices.reshape(views_n, 2, tile_n // 8, 2, 2),
        ("view",) + SUB,
    )
    return jax.shard_map(
        layer,
        mesh=fine,
        in_specs=(P("view", SUB, None), P(), P(), P(), P("view", None, None)),
        out_specs=P("view", SUB, None),
        check_vma=False,
    )
```

```python
import math

import jax
import jax.numpy as jnp
from jax import lax
from jax.experimental import pallas as pl
from jax.experimental.pallas import tpu as pltpu
from jax.sharding import Mesh

from jax.sharding import PartitionSpec as P

HEADS = 8
HD = 128
BLK = 128
NBLK = 16

SUB = ("zh", "zl", "yhi", "core")
HALF = ("zl", "yhi", "core")


def attention_kernel(epi_ref, flag_ref, q_ref, own_ref, anc_ref, anc2_ref, *rest):
    block = pl.program_id(0)
    slots = epi_ref.shape[1]
    other_refs, far_refs, o_ref = rest[:slots], rest[slots:-1], rest[-1]
    queries = q_ref[...]
    scale = math.sqrt(HD)

    def scores_of(keys):
        return lax.dot_general(
            queries, keys, (((1,), (1,)), ((), ())),
            preferred_element_type=jnp.float32,
        ) / scale

    own = own_ref[...]
    anc = anc_ref[...]
    anc2 = anc2_ref[...]
    parts = [
        (scores_of(own[:, :HD]), own[:, HD : 2 * HD]),
        (scores_of(anc[:, :HD]), anc[:, HD:]),
        (scores_of(anc2[:, :HD]), anc2[:, HD:]),
    ]
    for slot in range(slots):
        index = epi_ref[block, slot]
        use_other = (index < NBLK) == (flag_ref[0] == 1)
        keyvals = jnp.where(use_other, other_refs[slot][...], far_refs[slot][...])
        scores = jnp.where(index >= 0, scores_of(keyvals[:, :HD]), -jnp.inf)
        parts.append((scores, keyvals[:, HD:]))
    peak = parts[0][0].max(axis=1, keepdims=True)
    for scores, _ in parts[1:]:
        peak = jnp.maximum(peak, scores.max(axis=1, keepdims=True))
    total = None
    summed = None
    for scores, values in parts:
        raised = jnp.exp(scores - peak)
        row = raised.sum(axis=1, keepdims=True)
        prod = jnp.dot(raised.astype(jnp.bfloat16), values, preferred_element_type=jnp.float32)
        total = row if total is None else total + row
        summed = prod if summed is None else summed + prod
    o_ref[...] = (summed / total).astype(o_ref.dtype)


def attention(epi_rows, flags, resident, anchored, anchored2, other, far, rows):
    slots = epi_rows.shape[1]

    def spec_slot(slot):
        return pl.BlockSpec(
            (BLK, 2 * HD),
            lambda b, epi, flag: (jnp.clip(epi[b, slot], 0, 2 * NBLK - 1) % NBLK, 0),
        )

    return pl.pallas_call(
        attention_kernel,
        out_shape=jax.ShapeDtypeStruct((rows, HD), jnp.bfloat16),
        grid_spec=pltpu.PrefetchScalarGridSpec(
            num_scalar_prefetch=2,
            grid=(rows // BLK,),
            in_specs=[
                pl.BlockSpec((BLK, HD), lambda b, epi, flag: (flag[1] + b, 2)),
                pl.BlockSpec(resident.shape, lambda b, epi, flag: (0, 0)),
                pl.BlockSpec(anchored.shape, lambda b, epi, flag: (0, 0)),
                pl.BlockSpec(anchored2.shape, lambda b, epi, flag: (0, 0)),
            ]
            + [spec_slot(e) for e in range(slots)]
            + [spec_slot(e) for e in range(slots)],
            out_specs=pl.BlockSpec((BLK, HD), lambda b, epi, flag: (b, 0)),
        ),
    )(epi_rows, flags, resident, resident, anchored, anchored2, *([other] * slots), *([far] * slots))


def broadcast_view(value, root, count):
    me = lax.axis_index("view")
    dist = (me - root) % count
    held = jnp.where(dist == 0, value, jnp.zeros_like(value))
    reach = 0
    while 2 * reach + 1 < count:
        step = 2 * reach + 1
        up = lax.ppermute(held, "view", [(i, (i + step) % count) for i in range(count)])
        down = lax.ppermute(held, "view", [(i, (i - step) % count) for i in range(count)])
        lo = (dist >= reach + 1) & (dist <= reach + step)
        hi = (dist >= count - reach - step) & (dist <= count - reach - 1)
        held = jnp.where(lo, up, jnp.where(hi, down, held))
        reach += step
    return held


def layer(latents, qkv_weight, out_weight, anchor, epi_list):
    per_dev, tile_tokens, model_width = latents.shape
    views_n = lax.axis_size("view")
    half_n = lax.axis_size(HALF)
    tile_n = lax.axis_size(SUB)
    part_rows = tile_tokens * half_n
    core_n = lax.axis_size("core")
    slot = lax.axis_index("core")
    half = lax.axis_index("zh")

    target = anchor[0]
    anchor_latents = lax.dynamic_index_in_dim(latents, target % per_dev, 0, keepdims=False)
    anchor_latents = broadcast_view(anchor_latents, target // per_dev, views_n)

    flat = jnp.dot(
        latents.reshape(per_dev * tile_tokens, model_width), qkv_weight,
        preferred_element_type=jnp.float32,
    ).astype(jnp.bfloat16)
    projected = flat.reshape(per_dev, tile_tokens, HEADS, 3 * HD).transpose(2, 0, 1, 3)

    anchor_tile = jnp.dot(
        anchor_latents, qkv_weight, preferred_element_type=jnp.float32
    ).astype(jnp.bfloat16)
    anchor_tile = anchor_tile.reshape(tile_tokens, HEADS, 3 * HD)[..., HD:].transpose(1, 0, 2)

    def to_units(source):
        width = source.shape[-1]
        wide = jnp.broadcast_to(source[None], (tile_n // (HEADS * per_dev),) + source.shape)
        wide = wide.reshape(tile_n, tile_tokens, width)
        return lax.all_to_all(wide, SUB, 0, 0, tiled=True).reshape(tile_n * tile_tokens, width)

    resident = to_units(
        jnp.concatenate([projected[..., HD:], projected[..., :HD]], axis=-1).reshape(
            HEADS * per_dev, tile_tokens, 3 * HD
        )
    )
    halves = anchor_tile.reshape(HEADS * core_n, tile_tokens // core_n, 2 * HD)
    wide = jnp.broadcast_to(halves[None], (tile_n // (HEADS * core_n),) + halves.shape)
    wide = wide.reshape(tile_n, tile_tokens // core_n, 2 * HD)
    anchored = lax.all_to_all(wide, SUB, 0, 0, tiled=True).reshape(-1, 2 * HD)
    anchored2 = lax.ppermute(anchored, "core", [(0, 1), (1, 0)])

    other = lax.ppermute(resident, "core", [(0, 1), (1, 0)])
    pairs = []
    for v in range(views_n):
        for c in range(core_n):
            dest_view = (v + 1) % views_n if c == 1 else (v - 1) % views_n
            pairs.append((v * core_n + c, dest_view * core_n + (1 - c)))
    far = lax.ppermute(resident, ("view", "core"), pairs)
    epi_rows = lax.dynamic_index_in_dim(epi_list, slot, 0, keepdims=False)
    epi_rows = lax.dynamic_slice_in_dim(epi_rows, half * (part_rows // BLK), part_rows // BLK, 0)
    flags = jnp.stack([slot, half * (part_rows // BLK)]).astype(jnp.int32)
    attended = attention(epi_rows, flags, resident, anchored, anchored2, other, far, part_rows)
    attended = attended.reshape(half_n, tile_tokens, HD)
    returned = lax.all_to_all(attended, HALF, 0, 0, tiled=True)
    returned = returned.reshape(HEADS, per_dev, tile_tokens, HD)
    projected_out = jnp.einsum(
        "hvtc,hcd->vtd",
        returned,
        out_weight.reshape(HEADS, HD, model_width),
        preferred_element_type=jnp.float32,
    )
    return projected_out.astype(jnp.bfloat16)


def solution(mesh):
    views_n, tile_n = mesh.devices.shape
    fine = Mesh(
        mesh.devices.reshape(views_n, 2, tile_n // 8, 2, 2),
        ("view",) + SUB,
    )
    return jax.shard_map(
        layer,
        mesh=fine,
        in_specs=(P("view", SUB, None), P(), P(), P(), P("view", None, None)),
        out_specs=P("view", SUB, None),
        check_vma=False,
    )
```

```python
import math

import jax
import jax.numpy as jnp
from jax import lax
from jax.experimental import pallas as pl
from jax.experimental.pallas import tpu as pltpu
from jax.sharding import Mesh

from jax.sharding import PartitionSpec as P

HEADS = 8
HD = 128
BLK = 128
NBLK = 16

SUB = ("zh", "zl", "yhi", "core")
HALF = ("zl", "yhi", "core")


def attention_kernel(epi_ref, flag_ref, q_ref, own_ref, anc_ref, anc2_ref, *rest):
    block = pl.program_id(0)
    slots = epi_ref.shape[1]
    other_refs, far_refs, o_ref = rest[:slots], rest[slots:-1], rest[-1]
    queries = q_ref[...]
    scale = math.sqrt(HD)

    def scores_of(keys):
        return lax.dot_general(
            queries, keys, (((1,), (1,)), ((), ())),
            preferred_element_type=jnp.float32,
        ) / scale

    own = own_ref[...]
    anc = anc_ref[...]
    anc2 = anc2_ref[...]
    parts = [
        (scores_of(own[:, HD : 2 * HD]), own[:, 2 * HD :]),
        (scores_of(anc[:, :HD]), anc[:, HD:]),
        (scores_of(anc2[:, :HD]), anc2[:, HD:]),
    ]
    rows = queries.shape[0]
    nearby = []
    for slot in range(slots):
        index = epi_ref[block, slot]
        valid = index >= 0

        def slot_scores(slot=slot, index=index):
            use_other = (index < NBLK) == (flag_ref[0] == 1)
            keyvals = jnp.where(use_other, other_refs[slot][...], far_refs[slot][...])
            return scores_of(keyvals[:, :HD]), keyvals

        scores, keyvals = slot_scores()
        nearby.append((valid, jnp.where(valid, scores, -jnp.inf), keyvals))
    peak = parts[0][0].max(axis=1, keepdims=True)
    for scores, _ in parts[1:]:
        peak = jnp.maximum(peak, scores.max(axis=1, keepdims=True))
    for _, scores, _ in nearby:
        peak = jnp.maximum(peak, scores.max(axis=1, keepdims=True))
    total = None
    summed = None
    for scores, values in parts:
        raised = jnp.exp(scores - peak)
        row = raised.sum(axis=1, keepdims=True)
        prod = jnp.dot(raised.astype(jnp.bfloat16), values, preferred_element_type=jnp.float32)
        total = row if total is None else total + row
        summed = prod if summed is None else summed + prod
    for valid, scores, values in nearby:
        def slot_sums(scores=scores, values=values):
            raised = jnp.exp(scores - peak)
            return (
                raised.sum(axis=1, keepdims=True),
                jnp.dot(raised.astype(jnp.bfloat16), values[:, HD:], preferred_element_type=jnp.float32),
            )

        def no_sums():
            return jnp.zeros((rows, 1), jnp.float32), jnp.zeros((rows, HD), jnp.float32)

        row, prod = lax.cond(valid, slot_sums, no_sums)
        total = total + row
        summed = summed + prod
    o_ref[...] = (summed / total).astype(o_ref.dtype)


def attention(epi_rows, flags, resident, anchored, anchored2, other, far, rows):
    slots = epi_rows.shape[1]

    def spec_slot(slot):
        return pl.BlockSpec(
            (BLK, 2 * HD),
            lambda b, epi, flag: (jnp.clip(epi[b, slot], 0, 2 * NBLK - 1) % NBLK, 0),
        )

    return pl.pallas_call(
        attention_kernel,
        out_shape=jax.ShapeDtypeStruct((rows, HD), jnp.bfloat16),
        grid_spec=pltpu.PrefetchScalarGridSpec(
            num_scalar_prefetch=2,
            grid=(rows // BLK,),
            in_specs=[
                pl.BlockSpec((BLK, HD), lambda b, epi, flag: (flag[1] + b, 0)),
                pl.BlockSpec(resident.shape, lambda b, epi, flag: (0, 0)),
                pl.BlockSpec(anchored.shape, lambda b, epi, flag: (0, 0)),
                pl.BlockSpec(anchored2.shape, lambda b, epi, flag: (0, 0)),
            ]
            + [spec_slot(e) for e in range(slots)]
            + [spec_slot(e) for e in range(slots)],
            out_specs=pl.BlockSpec((BLK, HD), lambda b, epi, flag: (b, 0)),
        ),
    )(epi_rows, flags, resident, resident, anchored, anchored2, *([other] * slots), *([far] * slots))


def broadcast_view(value, root, count):
    me = lax.axis_index("view")
    dist = (me - root) % count
    held = jnp.where(dist == 0, value, jnp.zeros_like(value))
    reach = 0
    while 2 * reach + 1 < count:
        step = 2 * reach + 1
        up = lax.ppermute(held, "view", [(i, (i + step) % count) for i in range(count)])
        down = lax.ppermute(held, "view", [(i, (i - step) % count) for i in range(count)])
        lo = (dist >= reach + 1) & (dist <= reach + step)
        hi = (dist >= count - reach - step) & (dist <= count - reach - 1)
        held = jnp.where(lo, up, jnp.where(hi, down, held))
        reach += step
    return held


def layer(latents, qkv_weight, out_weight, anchor, epi_list):
    per_dev, tile_tokens, model_width = latents.shape
    views_n = lax.axis_size("view")
    half_n = lax.axis_size(HALF)
    tile_n = lax.axis_size(SUB)
    part_rows = tile_tokens * half_n
    core_n = lax.axis_size("core")
    slot = lax.axis_index("core")
    half = lax.axis_index("zh")

    target = anchor[0]
    anchor_latents = lax.dynamic_index_in_dim(latents, target % per_dev, 0, keepdims=False)
    anchor_latents = broadcast_view(anchor_latents, target // per_dev, views_n)

    flat = jnp.dot(
        latents.reshape(per_dev * tile_tokens, model_width), qkv_weight,
        preferred_element_type=jnp.float32,
    ).astype(jnp.bfloat16)
    projected = flat.reshape(per_dev, tile_tokens, HEADS, 3 * HD).transpose(2, 0, 1, 3)

    anchor_tile = jnp.dot(
        anchor_latents, qkv_weight, preferred_element_type=jnp.float32
    ).astype(jnp.bfloat16)
    anchor_tile = anchor_tile.reshape(tile_tokens, HEADS, 3 * HD)[..., HD:].transpose(1, 0, 2)

    def to_units(source):
        width = source.shape[-1]
        wide = jnp.broadcast_to(source[None], (tile_n // (HEADS * per_dev),) + source.shape)
        wide = wide.reshape(tile_n, tile_tokens, width)
        return lax.all_to_all(wide, SUB, 0, 0, tiled=True).reshape(tile_n * tile_tokens, width)

    resident = to_units(projected.reshape(HEADS * per_dev, tile_tokens, 3 * HD))
    own_kv = resident[:, HD:]
    halves = anchor_tile.reshape(HEADS * core_n, tile_tokens // core_n, 2 * HD)
    wide = jnp.broadcast_to(halves[None], (tile_n // (HEADS * core_n),) + halves.shape)
    wide = wide.reshape(tile_n, tile_tokens // core_n, 2 * HD)
    anchored = lax.all_to_all(wide, SUB, 0, 0, tiled=True).reshape(-1, 2 * HD)
    anchored2 = lax.ppermute(anchored, "core", [(0, 1), (1, 0)])

    other = lax.ppermute(own_kv, "core", [(0, 1), (1, 0)])
    pairs = []
    for v in range(views_n):
        for c in range(core_n):
            dest_view = (v + 1) % views_n if c == 1 else (v - 1) % views_n
            pairs.append((v * core_n + c, dest_view * core_n + (1 - c)))
    far = lax.ppermute(own_kv, ("view", "core"), pairs)
    epi_rows = lax.dynamic_index_in_dim(epi_list, slot, 0, keepdims=False)
    epi_rows = lax.dynamic_slice_in_dim(epi_rows, half * (part_rows // BLK), part_rows // BLK, 0)
    flags = jnp.stack([slot, half * (part_rows // BLK)]).astype(jnp.int32)
    attended = attention(epi_rows, flags, resident, anchored, anchored2, other, far, part_rows)
    attended = attended.reshape(half_n, tile_tokens, HD)
    returned = lax.all_to_all(attended, HALF, 0, 0, tiled=True)
    returned = returned.reshape(HEADS, per_dev, tile_tokens, HD)
    projected_out = jnp.einsum(
        "hvtc,hcd->vtd",
        returned,
        out_weight.reshape(HEADS, HD, model_width),
        preferred_element_type=jnp.float32,
    )
    return projected_out.astype(jnp.bfloat16)


def solution(mesh):
    views_n, tile_n = mesh.devices.shape
    fine = Mesh(
        mesh.devices.reshape(views_n, 2, tile_n // 8, 2, 2),
        ("view",) + SUB,
    )
    return jax.shard_map(
        layer,
        mesh=fine,
        in_specs=(P("view", SUB, None), P(), P(), P(), P("view", None, None)),
        out_specs=P("view", SUB, None),
        check_vma=False,
    )
```
